512 devices in a mesh: mem: 16 (over z_hi, y, core), gx: 32 (over x, z_lo).
Axes of the slice: x: 4, y: 4, z: 16 (z_hi: 2, z_lo: 8; z = z_hi * 8 + z_lo), core: 2. Of those that a mesh axis runs over, the one named last changes fastest.
Arguments:
- weights: bfloat16 [16, 512, 32768], P('mem', 'gx'), may hold values from -6 to 6
- perturbations: bfloat16 [2, 16, 512, 32768], P(None, 'mem', 'gx'), may hold values from -3 to 3
- obs_cell: int32 [131072], P('gx'), may hold values from 0 to 524287
- obs_slot: int32 [131072], P('gx'), may hold values from 0 to 1
- innovation: float32 [131072], P('gx'), may hold values from -24 to 24
- obs_weight: float32 [131072], P('gx'), may hold values from 0.5 to 4
- obs_count: int32 [32], P('gx'), may hold values from 2048 to 4096, as said below
Outputs:
- gradient: float32 [16, 512, 32768], P('mem', 'gx')
The draws below stay inside these ranges and needn't reach their ends.
Inputs may be any that keep to these rules, and one draw needn't show every extreme that they name: Slab s uses its first obs_count[s] observation slots, o = s * 4096 .. s * 4096 + obs_count[s] - 1; some slab is full and another holds 2048. `obs_cell`: the cell is numbered (x within the slab) * 512 * 64 + y * 64 + z; several observations may share a cell.
All inputs are finite; a program needn't handle non-finite values.
Results may differ from the reference program's by a relative error of at most 0.0029.
Values may be sent and summed in bfloat16 or wider, within the bound.
No kernel may reach another device: no remote copies, remote signals or barrier semaphores. Data moves between devices by JAX's collectives and lax.ppermute only.
A program may use at most 64 MiB of HBM per device.

```python
import math
import jax
import jax.numpy as jnp
from jax import lax

CX = 16
NY = 512
NZ = 64
TS = 2
OBS_DEV = 4096
MEMBERS = 16
NX = 512
SLABS = 32
NOBS = 131072


def draw_obs_count(key, part):
    first_key, second_key = jax.random.split(jax.random.fold_in(key, 17))
    base_counts = jax.random.randint(first_key, (SLABS,), OBS_DEV // 2, OBS_DEV + 1)
    full_slab = jax.random.randint(second_key, (), 0, SLABS)
    half_slab = (full_slab + 1) % SLABS
    positions = jnp.arange(SLABS)
    counts = jnp.where(positions == full_slab, OBS_DEV, base_counts)
    counts = jnp.where(positions == half_slab, OBS_DEV // 2, counts)
    return counts.astype(jnp.int32)


def set_ends(result, key, smallest, high):
    spot = [jax.random.randint(jax.random.fold_in(key, axis), (), 0, length) for axis, length in enumerate(result.shape)]
    longest = result.shape.index(max(result.shape))
    beside = spot[:longest] + [(spot[longest] + 1) % result.shape[longest]] + spot[longest + 1:]
    return result.at[tuple(spot)].set(smallest).at[tuple(beside)].set(high)


def block_scale(rng, extent, pieces, low, top_value):
    def one(axis_at, parts):
        steps = jax.random.uniform(jax.random.fold_in(jax.random.fold_in(rng, 6), axis_at), (parts,), jnp.float32, low / len(pieces), top_value / len(pieces))
        return jnp.repeat(jnp.exp(steps), extent[axis_at] // parts).reshape((-1,) + (1,) * (len(extent) - axis_at - 1))

    loudness = one(*pieces[0])
    for cut in pieces[1:]:
        loudness = loudness * one(*cut)
    return loudness


def centred(key, shape, scale, limit, cuts=(), dtype=jnp.bfloat16):
    gain = block_scale(key, shape, cuts, -0.22, 0.18) if cuts else 1.0
    entries = jax.random.normal(key, shape, jnp.float32) * scale * gain
    return jnp.minimum(jnp.maximum(entries, -limit), limit).astype(dtype)


def setup_inputs(seed: int = 0) -> dict:
    seeds = jax.random.split(jax.random.key(seed), 8)
    weights = centred(seeds[0], (MEMBERS, NX, NY * NZ), 1.0, 6.0, ((0, 16), (1, 32)))
    perturbations = centred(seeds[1], (TS, MEMBERS, NX, NY * NZ), 0.5, 3.0, ((1, 16), (2, 32)))
    obs_cell = set_ends(jax.random.randint(seeds[2], (NOBS,), 0, CX * NY * NZ), jax.random.fold_in(seeds[2], 1), 0, (CX * NY * NZ) - 1).astype(jnp.int32)
    obs_slot = set_ends(jax.random.randint(seeds[3], (NOBS,), 0, TS), jax.random.fold_in(seeds[3], 1), 0, TS - 1).astype(jnp.int32)
    innovation = centred(seeds[4], (NOBS,), 4.0, 24.0, ((0, 32),), jnp.float32)
    obs_weight = jnp.clip(jnp.exp(math.log(4.0) - 2.0794415 * jax.random.uniform(seeds[5], (NOBS,), jnp.float32) ** block_scale(seeds[5], (NOBS,), ((0, 32),), -0.2, 0.2)), 0.5, 4.0)
    obs_count = draw_obs_count(jax.random.fold_in(seeds[7], 71), 0)
    return {"weights": weights, "perturbations": perturbations, "obs_cell": obs_cell, "obs_slot": obs_slot, "innovation": innovation, "obs_weight": obs_weight, "obs_count": obs_count}


tap_reach = 15
corr_scale = 7.0

def tap_values():
    offsets = jnp.arange(-tap_reach, tap_reach + 1).astype(jnp.float32)
    bell = jnp.exp(-offsets * offsets / (2.0 * corr_scale * corr_scale))
    return (bell / jnp.sqrt(jnp.sum(bell * bell))).astype(jnp.bfloat16)

def square_band(count):
    positions = jnp.arange(count)
    offsets = positions[None, :] - positions[:, None]
    tap_table = tap_values()
    lookup = tap_table[jnp.clip(offsets + tap_reach, 0, 2 * tap_reach)]
    return jnp.where(jnp.abs(offsets) <= tap_reach, lookup, jnp.zeros_like(lookup))

def reference(weights, perturbations, obs_cell, obs_slot, innovation, obs_weight, obs_count):
    plane_cells = NY * NZ
    band_z = square_band(NZ).astype(jnp.float32)
    band_y = square_band(NY).astype(jnp.float32)
    tap_table = tap_values()

    def along_z(field):
        grid = field.reshape(NX, NY, NZ).astype(jnp.float32)
        return jnp.einsum('xyq,zq->xyz', grid, band_z).reshape(NX, plane_cells)

    def along_y(field):
        grid = field.reshape(NX, NY, NZ).astype(jnp.float32)
        return jnp.einsum('xqz,yq->xyz', grid, band_y).reshape(NX, plane_cells)

    def along_x(field):
        padded = jnp.pad(field.astype(jnp.float32), ((tap_reach, tap_reach), (0, 0)))
        running = jnp.zeros((NX, plane_cells), jnp.float32)
        for shift_index in range(2 * tap_reach + 1):
            running = running + tap_table[shift_index].astype(jnp.float32) * padded[shift_index:shift_index + NX]
        return running
    pert_members = jnp.moveaxis(perturbations, 1, 0)

    def forward(carry, item):
        weight_k, pert_k = item
        z_smooth = along_z(weight_k).astype(jnp.bfloat16)
        y_smooth = along_y(z_smooth).astype(jnp.bfloat16)
        smoothed = along_x(y_smooth)
        return (carry + pert_k.astype(jnp.float32) * smoothed[None], None)
    increment, _ = lax.scan(forward, jnp.zeros((TS, NX, plane_cells), jnp.float32), (weights, pert_members))
    obs_order = jnp.arange(NOBS).astype(jnp.int32)
    slab = obs_order // OBS_DEV
    rows = (slab * CX + obs_cell // plane_cells).astype(jnp.int32)
    columns = (obs_cell % plane_cells).astype(jnp.int32)
    live_mask = (obs_order % OBS_DEV < obs_count[slab]).astype(jnp.float32)
    sampled = increment[obs_slot, rows, columns]
    residual = live_mask * obs_weight * (sampled - innovation)
    forcing = jnp.zeros((TS, NX, plane_cells), jnp.float32).at[obs_slot, rows, columns].add(residual)

    def backward(item):
        weight_k, pert_k = item
        adjoint_source = lax.optimization_barrier(jnp.sum(pert_k.astype(jnp.float32) * forcing, axis=0)).astype(jnp.bfloat16)
        x_back = along_x(adjoint_source).astype(jnp.bfloat16)
        y_back = along_y(x_back).astype(jnp.bfloat16)
        return weight_k.astype(jnp.float32) + along_z(y_back)
    return lax.map(backward, (weights, pert_members))
```

```python
import numpy as np
import jax
import jax.numpy as jnp
from jax import lax
from jax.sharding import PartitionSpec as P

NY = 512
NZ = 64
LANES = 128


tap_reach = 15
corr_scale = 7.0


def padded_2(block, sides, width):
    for axis, dim in sides:
        count = lax.axis_size(axis)
        forward = [(i, i + 1) for i in range(count - 1)]
        backward = [(target, source) for source, target in forward]
        low = lax.ppermute(
            lax.slice_in_dim(block, block.shape[dim] - width, None, axis=dim), axis, forward
        )
        high = lax.ppermute(lax.slice_in_dim(block, 0, width, axis=dim), axis, backward)
        block = jnp.concatenate([low, block, high], axis=dim)
    return block


def tap_values():
    offsets = np.arange(-tap_reach, tap_reach + 1).astype(np.float32)
    bell = np.exp(-offsets * offsets / np.float32(2.0 * corr_scale * corr_scale)).astype(np.float32)
    taps = (bell / np.sqrt(np.sum(bell * bell, dtype=np.float32))).astype(np.float32)
    return taps.astype(jnp.bfloat16).astype(np.float32)


def band_matrix(count_out, count_in, start):
    out_pos = np.arange(count_out)
    in_pos = np.arange(count_in)
    offsets = in_pos[None, :] - out_pos[:, None] - start
    taps = tap_values()
    lookup = taps[np.clip(offsets + tap_reach, 0, 2 * tap_reach)]
    band = np.where(np.abs(offsets) <= tap_reach, lookup, np.zeros_like(lookup))
    return jnp.asarray(band.astype(jnp.bfloat16))


def along_z(field):
    members, slab_rows, plane_cells = field.shape
    band_z = band_matrix(NZ, NZ, 0)
    grid = field.reshape(members, slab_rows, NY, NZ)
    result = jnp.einsum("mxyq,zq->mxyz", grid, band_z, preferred_element_type=jnp.float32)
    return result.reshape(members, slab_rows, plane_cells)


def along_y(field):
    members, slab_rows, plane_cells = field.shape
    band_y = band_matrix(NY, NY, 0)
    grid = field.reshape(members, slab_rows, NY, NZ)
    result = jnp.einsum("mxqz,yq->mxyz", grid, band_y, preferred_element_type=jnp.float32)
    return result.reshape(members, slab_rows, plane_cells)


def along_x(padded, slab_rows):
    band_x = band_matrix(slab_rows, slab_rows + 2 * tap_reach, tap_reach)
    return jnp.einsum("ip,mpc->mic", band_x, padded, preferred_element_type=jnp.float32)


def local(weights, perturbations, obs_cell, obs_slot, innovation, obs_weight, obs_count):
    members, slab_rows, plane_cells = weights.shape
    slot_count = perturbations.shape[0]
    nobs = obs_cell.shape[0]
    rows = slab_rows * plane_cells // LANES
    z_smooth = along_z(weights).astype(jnp.bfloat16)
    y_smooth = along_y(z_smooth).astype(jnp.bfloat16)
    padded = padded_2(y_smooth, (("gx", 1),), tap_reach)
    smoothed = along_x(padded, slab_rows)

    obs_row = obs_cell // LANES
    lane_hit = lax.broadcasted_iota(jnp.int32, (nobs, LANES), 1) == (obs_cell % LANES)[:, None]
    s_rows = smoothed.reshape(rows, LANES)[obs_row]
    s_val = jnp.sum(jnp.where(lane_hit, s_rows, 0.0), axis=1)
    p_rows = perturbations.reshape(slot_count * rows, LANES)[obs_slot * rows + obs_row]
    p_val = jnp.sum(jnp.where(lane_hit, p_rows.astype(jnp.float32), 0.0), axis=1)
    sampled = lax.psum(p_val * s_val, "mem")

    live_mask = (jnp.arange(nobs) < obs_count[0]).astype(jnp.float32)
    residual = live_mask * obs_weight * (sampled - innovation)
    contrib = jnp.where(lane_hit, (p_val * residual)[:, None], 0.0)
    adjoint = jnp.zeros((rows, LANES), jnp.float32).at[obs_row].add(contrib)
    adjoint_source = adjoint.reshape(members, slab_rows, plane_cells).astype(jnp.bfloat16)

    padded_back = padded_2(adjoint_source, (("gx", 1),), tap_reach)
    x_back = along_x(padded_back, slab_rows).astype(jnp.bfloat16)
    y_back = along_y(x_back).astype(jnp.bfloat16)
    return weights.astype(jnp.float32) + along_z(y_back)


def solution(mesh):
    return jax.shard_map(
        local,
        mesh=mesh,
        in_specs=(
            P("mem", "gx", None),
            P(None, "mem", "gx", None),
            P("gx"),
            P("gx"),
            P("gx"),
            P("gx"),
            P("gx"),
        ),
        out_specs=P("mem", "gx", None),
        check_vma=False,
    )
```

```python
import numpy as np
import jax
import jax.numpy as jnp
from jax import lax
from jax.sharding import PartitionSpec as P

NY = 512
NZ = 64
LANES = 128


tap_reach = 15
corr_scale = 7.0


def padded_2(block, sides, width):
    for axis, dim in sides:
        count = lax.axis_size(axis)
        forward = [(i, i + 1) for i in range(count - 1)]
        backward = [(target, source) for source, target in forward]
        low = lax.ppermute(
            lax.slice_in_dim(block, block.shape[dim] - width, None, axis=dim), axis, forward
        )
        high = lax.ppermute(lax.slice_in_dim(block, 0, width, axis=dim), axis, backward)
        block = jnp.concatenate([low, block, high], axis=dim)
    return block


def tap_values():
    offsets = np.arange(-tap_reach, tap_reach + 1).astype(np.float32)
    bell = np.exp(-offsets * offsets / np.float32(2.0 * corr_scale * corr_scale)).astype(np.float32)
    taps = (bell / np.sqrt(np.sum(bell * bell, dtype=np.float32))).astype(np.float32)
    return taps.astype(jnp.bfloat16).astype(np.float32)


def band_matrix(count_out, count_in, start):
    out_pos = np.arange(count_out)
    in_pos = np.arange(count_in)
    offsets = in_pos[None, :] - out_pos[:, None] - start
    taps = tap_values()
    lookup = taps[np.clip(offsets + tap_reach, 0, 2 * tap_reach)]
    band = np.where(np.abs(offsets) <= tap_reach, lookup, np.zeros_like(lookup))
    return jnp.asarray(band.astype(jnp.bfloat16))


def along_z(field):
    members, slab_rows, plane_cells = field.shape
    band_z = band_matrix(NZ, NZ, 0)
    grid = field.reshape(members, slab_rows, NY, NZ)
    result = jnp.einsum("mxyq,zq->mxyz", grid, band_z, preferred_element_type=jnp.float32)
    return result.reshape(members, slab_rows, plane_cells)


def along_y(field):
    members, slab_rows, plane_cells = field.shape
    band_y = band_matrix(NY, NY, 0)
    grid = field.reshape(members, slab_rows, NY, NZ)
    result = jnp.einsum("mxqz,yq->mxyz", grid, band_y, preferred_element_type=jnp.float32)
    return result.reshape(members, slab_rows, plane_cells)


def along_x(padded, slab_rows):
    band_x = band_matrix(slab_rows, slab_rows + 2 * tap_reach, tap_reach)
    return jnp.einsum("ip,mpc->mic", band_x, padded, preferred_element_type=jnp.float32)


def butterfly_sum(value, axis):
    count = lax.axis_size(axis)
    step = 1
    while step < count:
        partner = lax.ppermute(value, axis, [(i, i ^ step) for i in range(count)])
        value = value + partner
        step *= 2
    return value


def local(weights, perturbations, obs_cell, obs_slot, innovation, obs_weight, obs_count):
    members, slab_rows, plane_cells = weights.shape
    slot_count = perturbations.shape[0]
    nobs = obs_cell.shape[0]
    rows = slab_rows * plane_cells // LANES
    z_smooth = along_z(weights).astype(jnp.bfloat16)
    y_smooth = along_y(z_smooth).astype(jnp.bfloat16)
    padded = padded_2(y_smooth, (("gx", 1),), tap_reach)
    smoothed = along_x(padded, slab_rows)

    obs_row = obs_cell // LANES
    lane_hit = lax.broadcasted_iota(jnp.int32, (nobs, LANES), 1) == (obs_cell % LANES)[:, None]
    s_rows = smoothed.reshape(rows, LANES)[obs_row]
    s_val = jnp.sum(jnp.where(lane_hit, s_rows, 0.0), axis=1)
    p_rows = perturbations.reshape(slot_count * rows, LANES)[obs_slot * rows + obs_row]
    p_val = jnp.sum(jnp.where(lane_hit, p_rows.astype(jnp.float32), 0.0), axis=1)
    sampled = butterfly_sum(p_val * s_val, "mem")

    live_mask = (jnp.arange(nobs) < obs_count[0]).astype(jnp.float32)
    residual = live_mask * obs_weight * (sampled - innovation)
    contrib = jnp.where(lane_hit, (p_val * residual)[:, None], 0.0)
    adjoint = jnp.zeros((rows, LANES), jnp.float32).at[obs_row].add(contrib)
    adjoint_source = adjoint.reshape(members, slab_rows, plane_cells).astype(jnp.bfloat16)

    padded_back = padded_2(adjoint_source, (("gx", 1),), tap_reach)
    x_back = along_x(padded_back, slab_rows).astype(jnp.bfloat16)
    y_back = along_y(x_back).astype(jnp.bfloat16)
    return weights.astype(jnp.float32) + along_z(y_back)


def solution(mesh):
    return jax.shard_map(
        local,
        mesh=mesh,
        in_specs=(
            P("mem", "gx", None),
            P(None, "mem", "gx", None),
            P("gx"),
            P("gx"),
            P("gx"),
            P("gx"),
            P("gx"),
        ),
        out_specs=P("mem", "gx", None),
        check_vma=False,
    )
```

```python
import numpy as np
import jax
import jax.numpy as jnp
from jax import lax
from jax.sharding import PartitionSpec as P
from jax.experimental import pallas as pl
from jax.experimental.pallas import tpu as pltpu

NY = 512
NZ = 64
LANES = 128


tap_reach = 15
corr_scale = 7.0


def padded_2(block, sides, width):
    for axis, dim in sides:
        count = lax.axis_size(axis)
        forward = [(i, i + 1) for i in range(count - 1)]
        backward = [(target, source) for source, target in forward]
        low = lax.ppermute(
            lax.slice_in_dim(block, block.shape[dim] - width, None, axis=dim), axis, forward
        )
        high = lax.ppermute(lax.slice_in_dim(block, 0, width, axis=dim), axis, backward)
        block = jnp.concatenate([low, block, high], axis=dim)
    return block


def tap_values():
    offsets = np.arange(-tap_reach, tap_reach + 1).astype(np.float32)
    bell = np.exp(-offsets * offsets / np.float32(2.0 * corr_scale * corr_scale)).astype(np.float32)
    taps = (bell / np.sqrt(np.sum(bell * bell, dtype=np.float32))).astype(np.float32)
    return taps.astype(jnp.bfloat16).astype(np.float32)


def band_matrix(count_out, count_in, start):
    out_pos = np.arange(count_out)
    in_pos = np.arange(count_in)
    offsets = in_pos[None, :] - out_pos[:, None] - start
    taps = tap_values()
    lookup = taps[np.clip(offsets + tap_reach, 0, 2 * tap_reach)]
    band = np.where(np.abs(offsets) <= tap_reach, lookup, np.zeros_like(lookup))
    return jnp.asarray(band.astype(jnp.bfloat16))


def along_z(field):
    members, slab_rows, plane_cells = field.shape
    band_z = band_matrix(NZ, NZ, 0)
    grid = field.reshape(members, slab_rows, NY, NZ)
    result = jnp.einsum("mxyq,zq->mxyz", grid, band_z, preferred_element_type=jnp.float32)
    return result.reshape(members, slab_rows, plane_cells)


def along_y(field):
    members, slab_rows, plane_cells = field.shape
    band_y = band_matrix(NY, NY, 0)
    grid = field.reshape(members, slab_rows, NY, NZ)
    result = jnp.einsum("mxqz,yq->mxyz", grid, band_y, preferred_element_type=jnp.float32)
    return result.reshape(members, slab_rows, plane_cells)


def along_x(padded, slab_rows):
    band_x = band_matrix(slab_rows, slab_rows + 2 * tap_reach, tap_reach)
    return jnp.einsum("ip,mpc->mic", band_x, padded, preferred_element_type=jnp.float32)


def butterfly_sum(value, axis):
    count = lax.axis_size(axis)
    step = 1
    while step < count:
        partner = lax.ppermute(value, axis, [(i, i ^ step) for i in range(count)])
        value = value + partner
        step *= 2
    return value


def gather_rows(index, field):
    count = index.shape[0]
    field_rows = field.shape[0]

    def kernel(index_ref, field_ref, out_ref):
        def body(i, carry):
            row = jnp.clip(index_ref[i], 0, field_rows - 1)
            out_ref[pl.ds(i, 1), :] = field_ref[pl.ds(row, 1), :]
            return carry

        lax.fori_loop(0, count, body, 0, unroll=8)

    return pl.pallas_call(
        kernel,
        out_shape=jax.ShapeDtypeStruct((count, LANES), field.dtype),
        grid_spec=pltpu.PrefetchScalarGridSpec(
            num_scalar_prefetch=1,
            grid=(1,),
            in_specs=[pl.BlockSpec(field.shape, lambda i, index: (0, 0))],
            out_specs=pl.BlockSpec((count, LANES), lambda i, index: (0, 0)),
        ),
        compiler_params=pltpu.CompilerParams(vmem_limit_bytes=40 * 1024 * 1024),
    )(index, field)


def scatter_regions(index, update, region_rows, splits):
    regions = len(region_rows)
    per_region = index.shape[0] // regions
    per_stream = per_region // splits
    total_rows = sum(region_rows)

    def kernel(index_ref, update_ref, out_ref, *accs):
        for acc in accs:
            acc[...] = jnp.zeros_like(acc)

        def body(j, carry):
            for region in range(regions):
                for split in range(splits):
                    i = region * per_region + split * per_stream + j
                    row = jnp.clip(index_ref[i], 0, region_rows[region])
                    acc = accs[region * splits + split]
                    acc[pl.ds(row, 1), :] += update_ref[pl.ds(i, 1), :]
            return carry

        lax.fori_loop(0, per_stream, body, 0, unroll=2)
        start = 0
        for region in range(regions):
            size = region_rows[region]
            total = accs[region * splits][0:size, :]
            for split in range(1, splits):
                total = total + accs[region * splits + split][0:size, :]
            out_ref[start:start + size, :] = total.astype(out_ref.dtype)
            start += size

    return pl.pallas_call(
        kernel,
        out_shape=jax.ShapeDtypeStruct((total_rows, LANES), jnp.bfloat16),
        grid_spec=pltpu.PrefetchScalarGridSpec(
            num_scalar_prefetch=1,
            grid=(1,),
            in_specs=[pl.BlockSpec(update.shape, lambda i, index: (0, 0))],
            out_specs=pl.BlockSpec((total_rows, LANES), lambda i, index: (0, 0)),
            scratch_shapes=[
                pltpu.VMEM((rows + 8, LANES), jnp.float32)
                for rows in region_rows
                for _ in range(splits)
            ],
        ),
        compiler_params=pltpu.CompilerParams(vmem_limit_bytes=48 * 1024 * 1024),
    )(index, update)


def neighbours(value, axis):
    count = lax.axis_size(axis)
    from_left = lax.ppermute(value, axis, [(i, i + 1) for i in range(count - 1)])
    from_right = lax.ppermute(value, axis, [(i + 1, i) for i in range(count - 1)])
    return from_left, from_right


def local(weights, perturbations, obs_cell, obs_slot, innovation, obs_weight, obs_count):
    members, slab_rows, plane_cells = weights.shape
    slot_count = perturbations.shape[0]
    nobs = obs_cell.shape[0]
    rows = slab_rows * plane_cells // LANES
    z_smooth = along_z(weights).astype(jnp.bfloat16)
    y_smooth = along_y(z_smooth).astype(jnp.bfloat16)
    padded = padded_2(y_smooth, (("gx", 1),), tap_reach)
    smoothed = along_x(padded, slab_rows)

    obs_row = obs_cell // LANES
    lane_hit = lax.broadcasted_iota(jnp.int32, (nobs, LANES), 1) == (obs_cell % LANES)[:, None]
    s_rows = gather_rows(obs_row, smoothed.reshape(rows, LANES))
    s_val = jnp.sum(jnp.where(lane_hit, s_rows, 0.0), axis=1)
    p_rows = perturbations.reshape(slot_count * rows, LANES)[obs_slot * rows + obs_row]
    p_val = jnp.sum(jnp.where(lane_hit, p_rows.astype(jnp.float32), 0.0), axis=1)
    sampled = butterfly_sum(p_val * s_val, "mem")

    live_mask = (jnp.arange(nobs) < obs_count[0]).astype(jnp.float32)
    residual = live_mask * obs_weight * (sampled - innovation)
    contrib = p_val * residual

    plane_rows = plane_cells // LANES
    halo_rows = tap_reach * plane_rows
    left_cell, right_cell = neighbours(obs_cell, "gx")
    left_contrib, right_contrib = neighbours(contrib, "gx")
    left_row = jnp.where(
        left_cell >= (slab_rows - tap_reach) * plane_cells,
        left_cell // LANES - (slab_rows - tap_reach) * plane_rows,
        halo_rows,
    )
    right_row = jnp.where(right_cell < tap_reach * plane_cells, right_cell // LANES, halo_rows)
    all_cell = jnp.concatenate([left_cell, obs_cell, right_cell])
    all_row = jnp.concatenate([left_row, obs_row, right_row])
    all_contrib = jnp.concatenate([left_contrib, contrib, right_contrib])
    all_hit = lax.broadcasted_iota(jnp.int32, (3 * nobs, LANES), 1) == (all_cell % LANES)[:, None]
    update = jnp.where(all_hit, all_contrib[:, None], 0.0)
    extended = scatter_regions(all_row, update, (halo_rows, rows, halo_rows), 2)
    padded_back = extended.reshape(members, slab_rows + 2 * tap_reach, plane_cells)
    x_back = along_x(padded_back, slab_rows).astype(jnp.bfloat16)
    y_back = along_y(x_back).astype(jnp.bfloat16)
    return weights.astype(jnp.float32) + along_z(y_back)


def solution(mesh):
    return jax.shard_map(
        local,
        mesh=mesh,
        in_specs=(
            P("mem", "gx", None),
            P(None, "mem", "gx", None),
            P("gx"),
            P("gx"),
            P("gx"),
            P("gx"),
            P("gx"),
        ),
        out_specs=P("mem", "gx", None),
        check_vma=False,
    )
```

```python
import numpy as np
import jax
import jax.numpy as jnp
from jax import lax
from jax.sharding import PartitionSpec as P
from jax.experimental import pallas as pl
from jax.experimental.pallas import tpu as pltpu

NY = 512
NZ = 64
LANES = 128


tap_reach = 15
corr_scale = 7.0


def padded_2(block, sides, width):
    for axis, dim in sides:
        count = lax.axis_size(axis)
        forward = [(i, i + 1) for i in range(count - 1)]
        backward = [(target, source) for source, target in forward]
        low = lax.ppermute(
            lax.slice_in_dim(block, block.shape[dim] - width, None, axis=dim), axis, forward
        )
        high = lax.ppermute(lax.slice_in_dim(block, 0, width, axis=dim), axis, backward)
        block = jnp.concatenate([low, block, high], axis=dim)
    return block


def tap_values():
    offsets = np.arange(-tap_reach, tap_reach + 1).astype(np.float32)
    bell = np.exp(-offsets * offsets / np.float32(2.0 * corr_scale * corr_scale)).astype(np.float32)
    taps = (bell / np.sqrt(np.sum(bell * bell, dtype=np.float32))).astype(np.float32)
    return taps.astype(jnp.bfloat16).astype(np.float32)


def band_matrix(count_out, count_in, start):
    out_pos = np.arange(count_out)
    in_pos = np.arange(count_in)
    offsets = in_pos[None, :] - out_pos[:, None] - start
    taps = tap_values()
    lookup = taps[np.clip(offsets + tap_reach, 0, 2 * tap_reach)]
    band = np.where(np.abs(offsets) <= tap_reach, lookup, np.zeros_like(lookup))
    return jnp.asarray(band.astype(jnp.bfloat16))


def along_z(field):
    members, slab_rows, plane_cells = field.shape
    band_z = band_matrix(NZ, NZ, 0)
    grid = field.reshape(members, slab_rows, NY, NZ)
    result = jnp.einsum("mxyq,zq->mxyz", grid, band_z, preferred_element_type=jnp.float32)
    return result.reshape(members, slab_rows, plane_cells)


def along_y(field):
    members, slab_rows, plane_cells = field.shape
    band_y = band_matrix(NY, NY, 0)
    grid = field.reshape(members, slab_rows, NY, NZ)
    result = jnp.einsum("mxqz,yq->mxyz", grid, band_y, preferred_element_type=jnp.float32)
    return result.reshape(members, slab_rows, plane_cells)


def along_x(padded, slab_rows):
    band_x = band_matrix(slab_rows, slab_rows + 2 * tap_reach, tap_reach)
    return jnp.einsum("ip,mpc->mic", band_x, padded, preferred_element_type=jnp.float32)


def butterfly_sum(value, axis):
    count = lax.axis_size(axis)
    step = 1
    while step < count:
        partner = lax.ppermute(value, axis, [(i, i ^ step) for i in range(count)])
        value = value + partner
        step *= 2
    return value


def gather_rows(index, field):
    count = index.shape[0]
    field_rows = field.shape[0]

    def kernel(index_ref, field_ref, out_ref):
        def body(i, carry):
            row = index_ref[i]
            out_ref[pl.ds(i, 1), :] = field_ref[pl.ds(row, 1), :]
            return carry

        lax.fori_loop(0, count, body, 0, unroll=8)

    return pl.pallas_call(
        kernel,
        out_shape=jax.ShapeDtypeStruct((count, LANES), field.dtype),
        grid_spec=pltpu.PrefetchScalarGridSpec(
            num_scalar_prefetch=1,
            grid=(1,),
            in_specs=[pl.BlockSpec(field.shape, lambda i, index: (0, 0))],
            out_specs=pl.BlockSpec((count, LANES), lambda i, index: (0, 0)),
        ),
        compiler_params=pltpu.CompilerParams(vmem_limit_bytes=40 * 1024 * 1024),
    )(index, field)


def scatter_regions(index, lane, value, region_rows, splits):
    regions = len(region_rows)
    per_region = index.shape[0] // regions
    per_stream = per_region // splits
    total_rows = sum(region_rows)

    def kernel(index_ref, lane_ref, value_ref, out_ref, *accs):
        for acc in accs:
            acc[...] = jnp.zeros_like(acc)
        lanes = lax.broadcasted_iota(jnp.int32, (1, LANES), 1)

        def body(j, carry):
            for region in range(regions):
                for split in range(splits):
                    i = region * per_region + split * per_stream + j
                    row = index_ref[i]
                    hit = jnp.where(lanes == lane_ref[i], value_ref[i], 0.0)
                    acc = accs[region * splits + split]
                    acc[pl.ds(row, 1), :] += hit
            return carry

        lax.fori_loop(0, per_stream, body, 0, unroll=2)
        start = 0
        for region in range(regions):
            size = region_rows[region]
            total = accs[region * splits][0:size, :]
            for split in range(1, splits):
                total = total + accs[region * splits + split][0:size, :]
            out_ref[start:start + size, :] = total.astype(out_ref.dtype)
            start += size

    return pl.pallas_call(
        kernel,
        out_shape=jax.ShapeDtypeStruct((total_rows, LANES), jnp.bfloat16),
        grid_spec=pltpu.PrefetchScalarGridSpec(
            num_scalar_prefetch=3,
            grid=(1,),
            in_specs=[],
            out_specs=pl.BlockSpec((total_rows, LANES), lambda i, *refs: (0, 0)),
            scratch_shapes=[
                pltpu.VMEM((rows + 8, LANES), jnp.float32)
                for rows in region_rows
                for _ in range(splits)
            ],
        ),
        compiler_params=pltpu.CompilerParams(vmem_limit_bytes=48 * 1024 * 1024),
    )(index, lane, value)


def neighbours(value, axis):
    count = lax.axis_size(axis)
    from_left = lax.ppermute(value, axis, [(i, i + 1) for i in range(count - 1)])
    from_right = lax.ppermute(value, axis, [(i + 1, i) for i in range(count - 1)])
    return from_left, from_right


def local(weights, perturbations, obs_cell, obs_slot, innovation, obs_weight, obs_count):
    members, slab_rows, plane_cells = weights.shape
    slot_count = perturbations.shape[0]
    nobs = obs_cell.shape[0]
    rows = slab_rows * plane_cells // LANES
    z_smooth = along_z(weights).astype(jnp.bfloat16)
    y_smooth = along_y(z_smooth).astype(jnp.bfloat16)
    padded = padded_2(y_smooth, (("gx", 1),), tap_reach)
    smoothed = along_x(padded, slab_rows)

    obs_row = jnp.clip(obs_cell // LANES, 0, rows - 1)
    lane_hit = lax.broadcasted_iota(jnp.int32, (nobs, LANES), 1) == (obs_cell % LANES)[:, None]
    s_rows = gather_rows(obs_row, smoothed.reshape(rows, LANES))
    s_val = jnp.sum(jnp.where(lane_hit, s_rows, 0.0), axis=1)
    p_rows = perturbations.reshape(slot_count * rows, LANES)[obs_slot * rows + obs_row]
    p_val = jnp.sum(jnp.where(lane_hit, p_rows.astype(jnp.float32), 0.0), axis=1)
    sampled = butterfly_sum(p_val * s_val, "mem")

    live_mask = (jnp.arange(nobs) < obs_count[0]).astype(jnp.float32)
    residual = live_mask * obs_weight * (sampled - innovation)
    contrib = p_val * residual

    plane_rows = plane_cells // LANES
    halo_rows = tap_reach * plane_rows
    late_cell, contrib = lax.optimization_barrier((obs_cell, contrib))
    left_cell, right_cell = neighbours(late_cell, "gx")
    left_contrib, right_contrib = neighbours(contrib, "gx")
    left_row = jnp.where(
        left_cell >= (slab_rows - tap_reach) * plane_cells,
        left_cell // LANES - (slab_rows - tap_reach) * plane_rows,
        halo_rows,
    )
    right_row = jnp.where(right_cell < tap_reach * plane_cells, right_cell // LANES, halo_rows)
    all_cell = jnp.concatenate([left_cell, obs_cell, right_cell])
    all_row = jnp.concatenate([
        jnp.clip(left_row, 0, halo_rows), obs_row, jnp.clip(right_row, 0, halo_rows)
    ])
    all_contrib = jnp.concatenate([left_contrib, contrib, right_contrib])
    extended = scatter_regions(
        all_row, all_cell % LANES, all_contrib, (halo_rows, rows, halo_rows), 2
    )
    padded_back = extended.reshape(members, slab_rows + 2 * tap_reach, plane_cells)
    x_back = along_x(padded_back, slab_rows).astype(jnp.bfloat16)
    y_back = along_y(x_back).astype(jnp.bfloat16)
    return weights.astype(jnp.float32) + along_z(y_back)


def solution(mesh):
    return jax.shard_map(
        local,
        mesh=mesh,
        in_specs=(
            P("mem", "gx", None),
            P(None, "mem", "gx", None),
            P("gx"),
            P("gx"),
            P("gx"),
            P("gx"),
            P("gx"),
        ),
        out_specs=P("mem", "gx", None),
        check_vma=False,
    )
```

```python
import numpy as np
import jax
import jax.numpy as jnp
from jax import lax
from jax.sharding import PartitionSpec as P
from jax.experimental import pallas as pl
from jax.experimental.pallas import tpu as pltpu

NY = 512
NZ = 64
LANES = 128


tap_reach = 15
corr_scale = 7.0


def padded_2(block, sides, width):
    for axis, dim in sides:
        count = lax.axis_size(axis)
        forward = [(i, i + 1) for i in range(count - 1)]
        backward = [(target, source) for source, target in forward]
        low = lax.ppermute(
            lax.slice_in_dim(block, block.shape[dim] - width, None, axis=dim), axis, forward
        )
        high = lax.ppermute(lax.slice_in_dim(block, 0, width, axis=dim), axis, backward)
        block = jnp.concatenate([low, block, high], axis=dim)
    return block


def tap_values():
    offsets = np.arange(-tap_reach, tap_reach + 1).astype(np.float32)
    bell = np.exp(-offsets * offsets / np.float32(2.0 * corr_scale * corr_scale)).astype(np.float32)
    taps = (bell / np.sqrt(np.sum(bell * bell, dtype=np.float32))).astype(np.float32)
    return taps.astype(jnp.bfloat16).astype(np.float32)


def band_matrix(count_out, count_in, start):
    out_pos = np.arange(count_out)
    in_pos = np.arange(count_in)
    offsets = in_pos[None, :] - out_pos[:, None] - start
    taps = tap_values()
    lookup = taps[np.clip(offsets + tap_reach, 0, 2 * tap_reach)]
    band = np.where(np.abs(offsets) <= tap_reach, lookup, np.zeros_like(lookup))
    return jnp.asarray(band.astype(jnp.bfloat16))


def along_z(field):
    members, slab_rows, plane_cells = field.shape
    band_z = band_matrix(NZ, NZ, 0)
    grid = field.reshape(members, slab_rows, NY, NZ)
    result = jnp.einsum("mxyq,zq->mxyz", grid, band_z, preferred_element_type=jnp.float32)
    return result.reshape(members, slab_rows, plane_cells)


def along_y(field):
    members, slab_rows, plane_cells = field.shape
    band_y = band_matrix(NY, NY, 0)
    grid = field.reshape(members, slab_rows, NY, NZ)
    result = jnp.einsum("mxqz,yq->mxyz", grid, band_y, preferred_element_type=jnp.float32)
    return result.reshape(members, slab_rows, plane_cells)


def along_x(padded, slab_rows):
    band_x = band_matrix(slab_rows, slab_rows + 2 * tap_reach, tap_reach)
    return jnp.einsum("ip,mpc->mic", band_x, padded, preferred_element_type=jnp.float32)


def group_sum(value, axis, bits):
    count = lax.axis_size(axis)
    codes = [0]
    for bit in bits:
        codes = codes + [code | (1 << bit) for code in codes]
    received = {0: value}
    for code in codes[1:]:
        received[code] = lax.ppermute(value, axis, [(i, i ^ code) for i in range(count)])
    own = lax.axis_index(axis) & sum(1 << bit for bit in bits)
    total = None
    for code in codes:
        term = received[code]
        for mine in codes[1:]:
            term = jnp.where(own == mine, received[code ^ mine], term)
        total = term if total is None else total + term
    return total


def butterfly_sum(value, axis):
    value = group_sum(value, axis, (0, 1))
    return group_sum(value, axis, (2, 3))


def gather_rows(index, field):
    count = index.shape[0]
    field_rows = field.shape[0]

    def kernel(index_ref, field_ref, out_ref):
        def body(i, carry):
            row = index_ref[i]
            out_ref[pl.ds(i, 1), :] = field_ref[pl.ds(row, 1), :]
            return carry

        lax.fori_loop(0, count, body, 0, unroll=8)

    return pl.pallas_call(
        kernel,
        out_shape=jax.ShapeDtypeStruct((count, LANES), field.dtype),
        grid_spec=pltpu.PrefetchScalarGridSpec(
            num_scalar_prefetch=1,
            grid=(1,),
            in_specs=[pl.BlockSpec(field.shape, lambda i, index: (0, 0))],
            out_specs=pl.BlockSpec((count, LANES), lambda i, index: (0, 0)),
        ),
        compiler_params=pltpu.CompilerParams(vmem_limit_bytes=40 * 1024 * 1024),
    )(index, field)


def scatter_regions(index, lane, value, region_rows, splits):
    regions = len(region_rows)
    per_region = index.shape[0] // regions
    per_stream = per_region // splits
    total_rows = sum(region_rows)

    def kernel(index_ref, lane_ref, value_ref, out_ref, *accs):
        for acc in accs:
            acc[...] = jnp.zeros_like(acc)
        lanes = lax.broadcasted_iota(jnp.int32, (1, LANES), 1)

        def body(j, carry):
            for region in range(regions):
                for split in range(splits):
                    i = region * per_region + split * per_stream + j
                    row = index_ref[i]
                    hit = jnp.where(lanes == lane_ref[i], value_ref[i], 0.0)
                    acc = accs[region * splits + split]
                    acc[pl.ds(row, 1), :] += hit
            return carry

        lax.fori_loop(0, per_stream, body, 0, unroll=2)
        start = 0
        for region in range(regions):
            size = region_rows[region]
            total = accs[region * splits][0:size, :]
            for split in range(1, splits):
                total = total + accs[region * splits + split][0:size, :]
            out_ref[start:start + size, :] = total.astype(out_ref.dtype)
            start += size

    return pl.pallas_call(
        kernel,
        out_shape=jax.ShapeDtypeStruct((total_rows, LANES), jnp.bfloat16),
        grid_spec=pltpu.PrefetchScalarGridSpec(
            num_scalar_prefetch=3,
            grid=(1,),
            in_specs=[],
            out_specs=pl.BlockSpec((total_rows, LANES), lambda i, *refs: (0, 0)),
            scratch_shapes=[
                pltpu.VMEM((rows + 8, LANES), jnp.float32)
                for rows in region_rows
                for _ in range(splits)
            ],
        ),
        compiler_params=pltpu.CompilerParams(vmem_limit_bytes=48 * 1024 * 1024),
    )(index, lane, value)


def neighbours(value, axis):
    count = lax.axis_size(axis)
    from_left = lax.ppermute(value, axis, [(i, i + 1) for i in range(count - 1)])
    from_right = lax.ppermute(value, axis, [(i + 1, i) for i in range(count - 1)])
    return from_left, from_right


def local(weights, perturbations, obs_cell, obs_slot, innovation, obs_weight, obs_count):
    members, slab_rows, plane_cells = weights.shape
    slot_count = perturbations.shape[0]
    nobs = obs_cell.shape[0]
    rows = slab_rows * plane_cells // LANES
    z_smooth = along_z(weights).astype(jnp.bfloat16)
    y_smooth = along_y(z_smooth).astype(jnp.bfloat16)
    padded = padded_2(y_smooth, (("gx", 1),), tap_reach)
    smoothed = along_x(padded, slab_rows)

    obs_row = jnp.clip(obs_cell // LANES, 0, rows - 1)
    lane_hit = lax.broadcasted_iota(jnp.int32, (nobs, LANES), 1) == (obs_cell % LANES)[:, None]
    s_rows = gather_rows(obs_row, smoothed.reshape(rows, LANES))
    s_val = jnp.sum(jnp.where(lane_hit, s_rows, 0.0), axis=1)
    p_rows = perturbations.reshape(slot_count * rows, LANES)[obs_slot * rows + obs_row]
    p_val = jnp.sum(jnp.where(lane_hit, p_rows.astype(jnp.float32), 0.0), axis=1)
    sampled = butterfly_sum(p_val * s_val, "mem")

    live_mask = (jnp.arange(nobs) < obs_count[0]).astype(jnp.float32)
    residual = live_mask * obs_weight * (sampled - innovation)
    contrib = p_val * residual

    plane_rows = plane_cells // LANES
    halo_rows = tap_reach * plane_rows
    late_cell, contrib = lax.optimization_barrier((obs_cell, contrib))
    left_cell, right_cell = neighbours(late_cell, "gx")
    left_contrib, right_contrib = neighbours(contrib, "gx")
    left_row = jnp.where(
        left_cell >= (slab_rows - tap_reach) * plane_cells,
        left_cell // LANES - (slab_rows - tap_reach) * plane_rows,
        halo_rows,
    )
    right_row = jnp.where(right_cell < tap_reach * plane_cells, right_cell // LANES, halo_rows)
    all_cell = jnp.concatenate([left_cell, obs_cell, right_cell])
    all_row = jnp.concatenate([
        jnp.clip(left_row, 0, halo_rows), obs_row, jnp.clip(right_row, 0, halo_rows)
    ])
    all_contrib = jnp.concatenate([left_contrib, contrib, right_contrib])
    extended = scatter_regions(
        all_row, all_cell % LANES, all_contrib, (halo_rows, rows, halo_rows), 2
    )
    padded_back = extended.reshape(members, slab_rows + 2 * tap_reach, plane_cells)
    x_back = along_x(padded_back, slab_rows).astype(jnp.bfloat16)
    y_back = along_y(x_back).astype(jnp.bfloat16)
    return weights.astype(jnp.float32) + along_z(y_back)


def solution(mesh):
    return jax.shard_map(
        local,
        mesh=mesh,
        in_specs=(
            P("mem", "gx", None),
            P(None, "mem", "gx", None),
            P("gx"),
            P("gx"),
            P("gx"),
            P("gx"),
            P("gx"),
        ),
        out_specs=P("mem", "gx", None),
        check_vma=False,
    )
```

```python
import numpy as np
import jax
import jax.numpy as jnp
from jax import lax
from jax.sharding import PartitionSpec as P
from jax.experimental import pallas as pl
from jax.experimental.pallas import tpu as pltpu

NY = 512
NZ = 64
LANES = 128


tap_reach = 15
corr_scale = 7.0


def padded_2(block, sides, width):
    for axis, dim in sides:
        count = lax.axis_size(axis)
        forward = [(i, i + 1) for i in range(count - 1)]
        backward = [(target, source) for source, target in forward]
        low = lax.ppermute(
            lax.slice_in_dim(block, block.shape[dim] - width, None, axis=dim), axis, forward
        )
        high = lax.ppermute(lax.slice_in_dim(block, 0, width, axis=dim), axis, backward)
        block = jnp.concatenate([low, block, high], axis=dim)
    return block


def tap_values():
    offsets = np.arange(-tap_reach, tap_reach + 1).astype(np.float32)
    bell = np.exp(-offsets * offsets / np.float32(2.0 * corr_scale * corr_scale)).astype(np.float32)
    taps = (bell / np.sqrt(np.sum(bell * bell, dtype=np.float32))).astype(np.float32)
    return taps.astype(jnp.bfloat16).astype(np.float32)


def band_matrix(count_out, count_in, start):
    out_pos = np.arange(count_out)
    in_pos = np.arange(count_in)
    offsets = in_pos[None, :] - out_pos[:, None] - start
    taps = tap_values()
    lookup = taps[np.clip(offsets + tap_reach, 0, 2 * tap_reach)]
    band = np.where(np.abs(offsets) <= tap_reach, lookup, np.zeros_like(lookup))
    return jnp.asarray(band.astype(jnp.bfloat16))


def along_z(field):
    members, slab_rows, plane_cells = field.shape
    band_z = band_matrix(NZ, NZ, 0)
    grid = field.reshape(members, slab_rows, NY, NZ)
    result = jnp.einsum("mxyq,zq->mxyz", grid, band_z, preferred_element_type=jnp.float32)
    return result.reshape(members, slab_rows, plane_cells)


def along_y(field):
    members, slab_rows, plane_cells = field.shape
    band_y = band_matrix(NY, NY, 0)
    grid = field.reshape(members, slab_rows, NY, NZ)
    result = jnp.einsum("mxqz,yq->mxyz", grid, band_y, preferred_element_type=jnp.float32)
    return result.reshape(members, slab_rows, plane_cells)


def along_x(padded, slab_rows):
    band_x = band_matrix(slab_rows, slab_rows + 2 * tap_reach, tap_reach)
    return jnp.einsum("ip,mpc->mic", band_x, padded, preferred_element_type=jnp.float32)


def butterfly_sum(value, axis):
    count = lax.axis_size(axis)
    step = 1
    while step < count:
        partner = lax.ppermute(value, axis, [(i, i ^ step) for i in range(count)])
        value = value + partner
        step *= 2
    return value


def gather_rows(index, field):
    count = index.shape[0]
    field_rows = field.shape[0]

    def kernel(index_ref, field_ref, out_ref):
        def body(i, carry):
            row = index_ref[i]
            out_ref[pl.ds(i, 1), :] = field_ref[pl.ds(row, 1), :]
            return carry

        lax.fori_loop(0, count, body, 0, unroll=8)

    return pl.pallas_call(
        kernel,
        out_shape=jax.ShapeDtypeStruct((count, LANES), field.dtype),
        grid_spec=pltpu.PrefetchScalarGridSpec(
            num_scalar_prefetch=1,
            grid=(1,),
            in_specs=[pl.BlockSpec(field.shape, lambda i, index: (0, 0))],
            out_specs=pl.BlockSpec((count, LANES), lambda i, index: (0, 0)),
        ),
        compiler_params=pltpu.CompilerParams(vmem_limit_bytes=40 * 1024 * 1024),
    )(index, field)


def scatter_regions(index, lane, value, region_rows, splits):
    regions = len(region_rows)
    per_region = index.shape[0] // regions
    per_stream = per_region // splits
    total_rows = sum(region_rows)

    def kernel(index_ref, lane_ref, value_ref, out_ref, *accs):
        for acc in accs:
            acc[...] = jnp.zeros_like(acc)
        lanes = lax.broadcasted_iota(jnp.int32, (1, LANES), 1)

        def body(j, carry):
            for region in range(regions):
                for split in range(splits):
                    i = region * per_region + split * per_stream + j
                    row = index_ref[i]
                    hit = jnp.where(lanes == lane_ref[i], value_ref[i], 0.0)
                    acc = accs[region * splits + split]
                    acc[pl.ds(row, 1), :] += hit
            return carry

        lax.fori_loop(0, per_stream, body, 0, unroll=2)
        start = 0
        for region in range(regions):
            size = region_rows[region]
            total = accs[region * splits][0:size, :]
            for split in range(1, splits):
                total = total + accs[region * splits + split][0:size, :]
            out_ref[start:start + size, :] = total.astype(out_ref.dtype)
            start += size

    return pl.pallas_call(
        kernel,
        out_shape=jax.ShapeDtypeStruct((total_rows, LANES), jnp.bfloat16),
        grid_spec=pltpu.PrefetchScalarGridSpec(
            num_scalar_prefetch=3,
            grid=(1,),
            in_specs=[],
            out_specs=pl.BlockSpec((total_rows, LANES), lambda i, *refs: (0, 0)),
            scratch_shapes=[
                pltpu.VMEM((rows + 8, LANES), jnp.float32)
                for rows in region_rows
                for _ in range(splits)
            ],
        ),
        compiler_params=pltpu.CompilerParams(vmem_limit_bytes=48 * 1024 * 1024),
    )(index, lane, value)


def neighbours(value, axis):
    count = lax.axis_size(axis)
    from_left = lax.ppermute(value, axis, [(i, i + 1) for i in range(count - 1)])
    from_right = lax.ppermute(value, axis, [(i + 1, i) for i in range(count - 1)])
    return from_left, from_right


def local(weights, perturbations, obs_cell, obs_slot, innovation, obs_weight, obs_count):
    members, slab_rows, plane_cells = weights.shape
    slot_count = perturbations.shape[0]
    nobs = obs_cell.shape[0]
    rows = slab_rows * plane_cells // LANES
    z_smooth = along_z(weights).astype(jnp.bfloat16)
    y_smooth = along_y(z_smooth).astype(jnp.bfloat16)
    padded = padded_2(y_smooth, (("gx", 1),), tap_reach)
    smoothed = along_x(padded, slab_rows)

    obs_row = jnp.clip(obs_cell // LANES, 0, rows - 1)
    lane_hit = lax.broadcasted_iota(jnp.int32, (nobs, LANES), 1) == (obs_cell % LANES)[:, None]
    s_rows = gather_rows(obs_row, smoothed.reshape(rows, LANES))
    s_val = jnp.sum(jnp.where(lane_hit, s_rows, 0.0), axis=1)
    p_rows = perturbations.reshape(slot_count * rows, LANES)[obs_slot * rows + obs_row]
    p_val = jnp.sum(jnp.where(lane_hit, p_rows.astype(jnp.float32), 0.0), axis=1)
    sampled = butterfly_sum(p_val * s_val, "mem")

    live_mask = (jnp.arange(nobs) < obs_count[0]).astype(jnp.float32)
    residual = live_mask * obs_weight * (sampled - innovation)
    contrib = p_val * residual

    plane_rows = plane_cells // LANES
    halo_rows = tap_reach * plane_rows
    late_cell, contrib = lax.optimization_barrier((obs_cell, contrib))
    left_cell, right_cell = neighbours(late_cell, "gx")
    left_contrib, right_contrib = neighbours(contrib, "gx")
    left_row = jnp.where(
        left_cell >= (slab_rows - tap_reach) * plane_cells,
        left_cell // LANES - (slab_rows - tap_reach) * plane_rows,
        halo_rows,
    )
    right_row = jnp.where(right_cell < tap_reach * plane_cells, right_cell // LANES, halo_rows)
    all_cell = jnp.concatenate([left_cell, obs_cell, right_cell])
    all_row = jnp.concatenate([
        jnp.clip(left_row, 0, halo_rows), obs_row, jnp.clip(right_row, 0, halo_rows)
    ])
    all_contrib = jnp.concatenate([left_contrib, contrib, right_contrib])
    extended = scatter_regions(
        all_row, all_cell % LANES, all_contrib, (halo_rows, rows, halo_rows), 4
    )
    padded_back = extended.reshape(members, slab_rows + 2 * tap_reach, plane_cells)
    x_back = along_x(padded_back, slab_rows).astype(jnp.bfloat16)
    y_back = along_y(x_back).astype(jnp.bfloat16)
    return weights.astype(jnp.float32) + along_z(y_back)


def solution(mesh):
    return jax.shard_map(
        local,
        mesh=mesh,
        in_specs=(
            P("mem", "gx", None),
            P(None, "mem", "gx", None),
            P("gx"),
            P("gx"),
            P("gx"),
            P("gx"),
            P("gx"),
        ),
        out_specs=P("mem", "gx", None),
        check_vma=False,
    )
```

```python
import numpy as np
import jax
import jax.numpy as jnp
from jax import lax
from jax.sharding import PartitionSpec as P
from jax.experimental import pallas as pl
from jax.experimental.pallas import tpu as pltpu

NY = 512
NZ = 64
LANES = 128


tap_reach = 15
corr_scale = 7.0


def padded_2(block, sides, width):
    for axis, dim in sides:
        count = lax.axis_size(axis)
        forward = [(i, i + 1) for i in range(count - 1)]
        backward = [(target, source) for source, target in forward]
        low = lax.ppermute(
            lax.slice_in_dim(block, block.shape[dim] - width, None, axis=dim), axis, forward
        )
        high = lax.ppermute(lax.slice_in_dim(block, 0, width, axis=dim), axis, backward)
        block = jnp.concatenate([low, block, high], axis=dim)
    return block


def tap_values():
    offsets = np.arange(-tap_reach, tap_reach + 1).astype(np.float32)
    bell = np.exp(-offsets * offsets / np.float32(2.0 * corr_scale * corr_scale)).astype(np.float32)
    taps = (bell / np.sqrt(np.sum(bell * bell, dtype=np.float32))).astype(np.float32)
    return taps.astype(jnp.bfloat16).astype(np.float32)


def band_matrix(count_out, count_in, start):
    out_pos = np.arange(count_out)
    in_pos = np.arange(count_in)
    offsets = in_pos[None, :] - out_pos[:, None] - start
    taps = tap_values()
    lookup = taps[np.clip(offsets + tap_reach, 0, 2 * tap_reach)]
    band = np.where(np.abs(offsets) <= tap_reach, lookup, np.zeros_like(lookup))
    return jnp.asarray(band.astype(jnp.bfloat16))


def along_z(field):
    members, slab_rows, plane_cells = field.shape
    band_z = band_matrix(NZ, NZ, 0)
    grid = field.reshape(members, slab_rows, NY, NZ)
    result = jnp.einsum("mxyq,zq->mxyz", grid, band_z, preferred_element_type=jnp.float32)
    return result.reshape(members, slab_rows, plane_cells)


def along_y(field):
    members, slab_rows, plane_cells = field.shape
    band_y = band_matrix(NY, NY, 0)
    grid = field.reshape(members, slab_rows, NY, NZ)
    result = jnp.einsum("mxqz,yq->mxyz", grid, band_y, preferred_element_type=jnp.float32)
    return result.reshape(members, slab_rows, plane_cells)


def along_x(padded, slab_rows):
    band_x = band_matrix(slab_rows, slab_rows + 2 * tap_reach, tap_reach)
    return jnp.einsum("ip,mpc->mic", band_x, padded, preferred_element_type=jnp.float32)


def butterfly_sum(value, axis):
    count = lax.axis_size(axis)
    step = 1
    while step < count:
        partner = lax.ppermute(value, axis, [(i, i ^ step) for i in range(count)])
        value = value + partner
        step *= 2
    return value


def gather_rows(index, field):
    count = index.shape[0]
    field_rows = field.shape[0]

    def kernel(index_ref, field_ref, out_ref):
        def body(i, carry):
            row = index_ref[i]
            out_ref[pl.ds(i, 1), :] = field_ref[pl.ds(row, 1), :]
            return carry

        lax.fori_loop(0, count, body, 0, unroll=8)

    return pl.pallas_call(
        kernel,
        out_shape=jax.ShapeDtypeStruct((count, LANES), field.dtype),
        grid_spec=pltpu.PrefetchScalarGridSpec(
            num_scalar_prefetch=1,
            grid=(1,),
            in_specs=[pl.BlockSpec(field.shape, lambda i, index: (0, 0))],
            out_specs=pl.BlockSpec((count, LANES), lambda i, index: (0, 0)),
        ),
        compiler_params=pltpu.CompilerParams(vmem_limit_bytes=40 * 1024 * 1024),
    )(index, field)


def scatter_regions(index, value, region_rows, splits):
    regions = len(region_rows)
    per_region = index.shape[0] // regions
    per_stream = per_region // splits
    total_rows = sum(region_rows)

    def kernel(index_ref, value_ref, out_ref, *accs):
        for acc in accs:
            acc[...] = jnp.zeros_like(acc)
        lanes = lax.broadcasted_iota(jnp.int32, (1, LANES), 1)

        def body(j, carry):
            for region in range(regions):
                for split in range(splits):
                    i = region * per_region + split * per_stream + j
                    code = index_ref[i]
                    row = code // LANES
                    hit = jnp.where(lanes == code % LANES, value_ref[i], 0.0)
                    acc = accs[region * splits + split]
                    acc[pl.ds(row, 1), :] += hit
            return carry

        lax.fori_loop(0, per_stream, body, 0, unroll=2)
        start = 0
        for region in range(regions):
            size = region_rows[region]
            total = accs[region * splits][0:size, :]
            for split in range(1, splits):
                total = total + accs[region * splits + split][0:size, :]
            out_ref[start:start + size, :] = total.astype(out_ref.dtype)
            start += size

    return pl.pallas_call(
        kernel,
        out_shape=jax.ShapeDtypeStruct((total_rows, LANES), jnp.bfloat16),
        grid_spec=pltpu.PrefetchScalarGridSpec(
            num_scalar_prefetch=2,
            grid=(1,),
            in_specs=[],
            out_specs=pl.BlockSpec((total_rows, LANES), lambda i, *refs: (0, 0)),
            scratch_shapes=[
                pltpu.VMEM((rows + 8, LANES), jnp.float32)
                for rows in region_rows
                for _ in range(splits)
            ],
        ),
        compiler_params=pltpu.CompilerParams(vmem_limit_bytes=48 * 1024 * 1024),
    )(index, value)


def neighbours(value, axis):
    count = lax.axis_size(axis)
    from_left = lax.ppermute(value, axis, [(i, i + 1) for i in range(count - 1)])
    from_right = lax.ppermute(value, axis, [(i + 1, i) for i in range(count - 1)])
    return from_left, from_right


def local(weights, perturbations, obs_cell, obs_slot, innovation, obs_weight, obs_count):
    members, slab_rows, plane_cells = weights.shape
    slot_count = perturbations.shape[0]
    nobs = obs_cell.shape[0]
    rows = slab_rows * plane_cells // LANES
    z_smooth = along_z(weights).astype(jnp.bfloat16)
    y_smooth = along_y(z_smooth).astype(jnp.bfloat16)
    padded = padded_2(y_smooth, (("gx", 1),), tap_reach)
    smoothed = along_x(padded, slab_rows)

    obs_row = jnp.clip(obs_cell // LANES, 0, rows - 1)
    lane_hit = lax.broadcasted_iota(jnp.int32, (nobs, LANES), 1) == (obs_cell % LANES)[:, None]
    s_rows = gather_rows(obs_row, smoothed.reshape(rows, LANES))
    s_val = jnp.sum(jnp.where(lane_hit, s_rows, 0.0), axis=1)
    p_rows = perturbations.reshape(slot_count * rows, LANES)[obs_slot * rows + obs_row]
    p_val = jnp.sum(jnp.where(lane_hit, p_rows.astype(jnp.float32), 0.0), axis=1)
    sampled = butterfly_sum(p_val * s_val, "mem")

    live_mask = (jnp.arange(nobs) < obs_count[0]).astype(jnp.float32)
    residual = live_mask * obs_weight * (sampled - innovation)
    contrib = p_val * residual

    plane_rows = plane_cells // LANES
    halo_rows = tap_reach * plane_rows
    late_cell, contrib = lax.optimization_barrier((obs_cell, contrib))
    left_cell, right_cell = neighbours(late_cell, "gx")
    left_contrib, right_contrib = neighbours(contrib, "gx")
    left_row = jnp.where(
        left_cell >= (slab_rows - tap_reach) * plane_cells,
        left_cell // LANES - (slab_rows - tap_reach) * plane_rows,
        halo_rows,
    )
    right_row = jnp.where(right_cell < tap_reach * plane_cells, right_cell // LANES, halo_rows)
    all_cell = jnp.concatenate([left_cell, obs_cell, right_cell])
    all_row = jnp.concatenate([
        jnp.clip(left_row, 0, halo_rows), obs_row, jnp.clip(right_row, 0, halo_rows)
    ])
    all_contrib = jnp.concatenate([left_contrib, contrib, right_contrib])
    extended = scatter_regions(
        all_row * LANES + all_cell % LANES, all_contrib, (halo_rows, rows, halo_rows), 4
    )
    padded_back = extended.reshape(members, slab_rows + 2 * tap_reach, plane_cells)
    x_back = along_x(padded_back, slab_rows).astype(jnp.bfloat16)
    y_back = along_y(x_back).astype(jnp.bfloat16)
    return weights.astype(jnp.float32) + along_z(y_back)


def solution(mesh):
    return jax.shard_map(
        local,
        mesh=mesh,
        in_specs=(
            P("mem", "gx", None),
            P(None, "mem", "gx", None),
            P("gx"),
            P("gx"),
            P("gx"),
            P("gx"),
            P("gx"),
        ),
        out_specs=P("mem", "gx", None),
        check_vma=False,
    )
```
